256 devices in a mesh: rep: 16 (over z_lo, x), shard: 16 (over z_hi, y, core).
Axes of the slice: x: 4, y: 4, z: 8 (z_hi: 2, z_lo: 4; z = z_hi * 4 + z_lo), core: 2. Of those that a mesh axis runs over, the one named last changes fastest.
Arguments:
- attn: bfloat16 [16, 6144, 2560], P('rep', 'shard'), may hold values from -6 to 6
- resid: bfloat16 [16, 6144, 2560], P('rep', 'shard'), may hold values from -200 to 200
- cotangent: bfloat16 [16, 6144, 2560], P('rep', 'shard'), may hold values from -6 to 6
- gain: float32 [2560], replicated, may hold values from 0.1 to 1.9
- numer: float32 [16, 2560, 2560], P('rep', 'shard'), may hold values from -6 to 6
- pweight: float32 [16], P('rep'), may hold values from 0.5 to 2
- round_bit: int32 [1], replicated, may hold values from 0 to 3
Outputs:
- new_numer: float32 [16, 2560, 2560], P('rep', 'shard')
- new_pweight: float32 [16], P('rep')
The draws below stay inside these ranges and needn't reach their ends.
All inputs are finite; a program needn't handle non-finite values.
Results may differ from the reference program's by a relative error of at most 0.008.
Values may be sent and summed in bfloat16 or wider, within the bound.
No kernel may reach another device: no remote copies, remote signals or barrier semaphores. Data moves between devices by JAX's collectives and lax.ppermute only.
A program may use at most 192 MiB of HBM per device.

```python
import math
import jax
import jax.numpy as jnp
from jax import lax

DIN = 2560
DOUT = 2560
TOK_DEV = 384
TOKENS = 6144
BITS = 4
N_REP = 16
N_SHARD = 16


def raised(drawn, own_key, source, target, parts, factor):
    def block_of(dim):
        return (jnp.arange(drawn.shape[dim]) // (drawn.shape[dim] // parts)).reshape((-1,) + (1,) * (drawn.ndim - 1 - dim))

    one_side = jax.random.permutation(own_key, parts)[block_of(target)]
    far = (block_of(target) + parts // 2) % parts
    return jnp.where((block_of(source) == one_side) | (block_of(source) == far), factor * drawn, drawn)


def level_of(key, shape, shards, smallest, top_value):
    def one(position, blocks):
        draws = jax.random.uniform(jax.random.fold_in(jax.random.fold_in(key, 6), position), (blocks,), jnp.float32, smallest / len(shards), top_value / len(shards))
        return jnp.repeat(jnp.exp(draws), shape[position] // blocks).reshape((-1,) + (1,) * (len(shape) - position - 1))

    factor_of = one(*shards[0])
    for cut in shards[1:]:
        factor_of = factor_of * one(*cut)
    return factor_of


def bell_draw(key, dims, spread, bound, split=(), kind=jnp.bfloat16):
    level = level_of(key, dims, split, -0.22, 0.18) if split else 1.0
    values = jax.random.normal(key, dims, jnp.float32) * spread * level
    return jnp.minimum(jnp.maximum(values, -bound), bound).astype(kind)


def heavy_noise(own_key, shape, deviation, reach, shards, heavy, held_as=jnp.bfloat16):
    result = deviation * jax.random.normal(own_key, shape, jnp.float32)
    if shards:
        result = result * level_of(own_key, shape, shards, -0.22, 0.18)
    return jnp.clip(raised(result, jax.random.fold_in(own_key, 3), *heavy), -reach, reach).astype(held_as)


def setup_inputs(seed: int = 0) -> dict:
    streams_of = jax.random.split(jax.random.key(seed), 8)
    return {
        "attn": heavy_noise(streams_of[0], (N_REP, TOKENS, DIN), 1.0, 6.0, ((0, 16), (1, 16)), (1, 2, 16, 2.0)),
        "resid": bell_draw(streams_of[1], (N_REP, TOKENS, DOUT), 40.0, 200.0, ((0, 16), (1, 16))),
        "cotangent": bell_draw(streams_of[2], (N_REP, TOKENS, DOUT), 1.0, 6.0, ((0, 16), (1, 16))),
        "gain": jnp.clip(1.0 + 0.18 * jax.random.normal(streams_of[3], (DOUT,), jnp.float32), 0.1, 1.9),
        "numer": bell_draw(streams_of[4], (N_REP, DIN, DOUT), 1.0, 6.0, ((0, 16), (1, 16)), jnp.float32),
        "pweight": jnp.clip(jnp.exp(math.log(2.0) - 1.3862944 * jax.random.uniform(streams_of[5], (N_REP,), jnp.float32) ** level_of(streams_of[5], (N_REP,), ((0, 16),), -0.2, 0.2)), 0.5, 2.0),
        "round_bit": jax.random.randint(streams_of[6], (1,), 0, BITS).astype(jnp.int32),
    }


EPS = 1e-05
learning_rate = 0.5

def replica_step(item):
    attn_r, resid_r, cot_r, numer_r, weight_r, gain = item
    weights = (numer_r / weight_r).astype(jnp.bfloat16)
    pre = resid_r.astype(jnp.float32) + jnp.dot(attn_r, weights, preferred_element_type=jnp.float32)
    inv = lax.rsqrt(lax.optimization_barrier(jnp.mean(pre * pre, axis=1, keepdims=True)) + EPS)
    normed = pre * inv
    dnorm = cot_r.astype(jnp.float32) * gain
    dpre = (inv * (dnorm - normed * lax.optimization_barrier(jnp.mean(dnorm * normed, axis=1, keepdims=True)))).astype(jnp.bfloat16)
    groups_a = attn_r.reshape(N_SHARD, TOK_DEV, DIN)
    groups_d = dpre.reshape(N_SHARD, TOK_DEV, DOUT)

    def add_group(total, pair):
        part = jnp.dot(pair[0].T, pair[1], preferred_element_type=jnp.float32)
        return (total + part.astype(jnp.bfloat16).astype(jnp.float32), None)
    grad, _ = lax.scan(add_group, jnp.zeros((DIN, DOUT), jnp.float32), (groups_a, groups_d))
    return numer_r - learning_rate * grad

def reference(attn, resid, cotangent, gain, numer, pweight, round_bit):
    gains = jnp.broadcast_to(gain, (N_REP, DOUT))
    stepped = lax.map(replica_step, (attn, resid, cotangent, numer, pweight, gains))
    partner = jnp.bitwise_xor(jnp.arange(N_REP, dtype=jnp.int32), jnp.left_shift(jnp.int32(1), round_bit[0].astype(jnp.int32)))
    new_numer = 0.5 * (stepped + stepped[partner])
    new_pweight = 0.5 * (pweight + pweight[partner])
    return (new_numer, new_pweight)
```

```python
import jax
import jax.numpy as jnp
import numpy as np
from jax import lax
from jax.sharding import Mesh, PartitionSpec as P

EPS = 1e-05
learning_rate = 0.5


def shortened(shard):

    def short(part):
        return part.astype(jnp.bfloat16) if part.dtype == jnp.float32 else part

    return jax.tree.map(short, shard)


def from_partner(shard, axis, apart):
    return lax.ppermute(shard, axis, [(i, i ^ 1 << apart) for i in range(lax.axis_size(axis))])


def on_device(attn, resid, cotangent, gain, numer, pweight, round_bit):
    n_sh = lax.axis_size("sh")
    n_core = lax.axis_size("core")
    acts = attn[0]
    tok, din = acts.shape
    rows = din // (n_sh * n_core)
    weight_rows = (numer[0] / pweight[0]).astype(jnp.bfloat16)
    me = lax.axis_index("core")
    other = [(i, i ^ 1) for i in range(n_core)]
    w_own = lax.all_gather(weight_rows, "sh", axis=0, tiled=False)
    w_other = lax.ppermute(w_own, "core", other)
    acts4 = acts.reshape(tok, n_sh, n_core, rows)
    a_own = lax.dynamic_index_in_dim(acts4, me, axis=2, keepdims=False)
    a_other = lax.dynamic_index_in_dim(acts4, 1 - me, axis=2, keepdims=False)
    pre = (
        resid[0].astype(jnp.float32)
        + jnp.einsum("tsi,sio->to", a_own, w_own, preferred_element_type=jnp.float32)
        + jnp.einsum("tsi,sio->to", a_other, w_other, preferred_element_type=jnp.float32)
    )
    inv = lax.rsqrt(jnp.mean(pre * pre, axis=1, keepdims=True) + EPS)
    normed = pre * inv
    dnorm = cotangent[0].astype(jnp.float32) * gain
    dpre = (inv * (dnorm - normed * jnp.mean(dnorm * normed, axis=1, keepdims=True))).astype(
        jnp.bfloat16
    )
    part_other = jnp.einsum(
        "tsi,to->sio", a_other, dpre, preferred_element_type=jnp.float32
    ).astype(jnp.bfloat16)
    part_own = jnp.einsum(
        "tsi,to->sio", a_own, dpre, preferred_element_type=jnp.float32
    ).astype(jnp.bfloat16)
    part = part_own + lax.ppermute(part_other, "core", other)
    grad = lax.psum_scatter(part, "sh", scatter_dimension=0, tiled=False).astype(jnp.float32)
    stepped = numer[0] - learning_rate * grad
    levels = lax.axis_size("rep").bit_length() - 1

    def pushed(bit):

        def send_pair(pair):
            return jax.tree.map(
                lambda part, own: part.astype(own.dtype),
                from_partner(shortened(pair), "rep", bit),
                pair,
            )

        return send_pair

    other_numer, other_weight = lax.switch(
        round_bit[0], [pushed(level) for level in range(levels)], (stepped, pweight)
    )
    new_numer = (0.5 * (stepped + other_numer))[None]
    new_pweight = 0.5 * (pweight + other_weight)
    return (new_numer, new_pweight)


def solution(mesh):
    n_rep, n_shard = mesh.devices.shape
    devices = np.asarray(mesh.devices).reshape(n_rep, n_shard // 2, 2)
    split = Mesh(devices, ("rep", "sh", "core"))
    rows = P("rep", ("sh", "core"), None)
    in_specs = (rows, rows, rows, P(), rows, P("rep"), P())
    out_specs = (rows, P("rep"))
    return jax.shard_map(
        on_device, mesh=split, in_specs=in_specs, out_specs=out_specs, check_vma=False
    )
```

```python
import jax
import jax.numpy as jnp
import numpy as np
from jax import lax
from jax.sharding import Mesh, PartitionSpec as P

EPS = 1e-05
learning_rate = 0.5


def shortened(shard):

    def short(part):
        return part.astype(jnp.bfloat16) if part.dtype == jnp.float32 else part

    return jax.tree.map(short, shard)


def from_partner(shard, axis, apart):
    return lax.ppermute(shard, axis, [(i, i ^ 1 << apart) for i in range(lax.axis_size(axis))])


def on_device(attn, resid, cotangent, gain, numer, pweight, round_bit):
    n_zh = lax.axis_size("zh")
    n_y = lax.axis_size("y")
    n_core = lax.axis_size("core")
    acts = attn[0]
    tok, din = acts.shape
    rows = din // (n_zh * n_y * n_core)
    weight_rows = (numer[0] / pweight[0]).astype(jnp.bfloat16)
    me = lax.axis_index("core")
    other = [(i, i ^ 1) for i in range(n_core)]
    w_z = lax.all_gather(weight_rows, "zh", axis=0, tiled=False)
    w_own = lax.all_gather(w_z, "y", axis=0, tiled=False)
    w_other = lax.ppermute(w_own, "core", other)
    acts5 = acts.reshape(tok, n_zh, n_y, n_core, rows)
    a_own = lax.dynamic_index_in_dim(acts5, me, axis=3, keepdims=False)
    a_other = lax.dynamic_index_in_dim(acts5, 1 - me, axis=3, keepdims=False)
    pre = (
        resid[0].astype(jnp.float32)
        + jnp.einsum("tzyi,yzio->to", a_own, w_own, preferred_element_type=jnp.float32)
        + jnp.einsum("tzyi,yzio->to", a_other, w_other, preferred_element_type=jnp.float32)
    )
    inv = lax.rsqrt(jnp.mean(pre * pre, axis=1, keepdims=True) + EPS)
    normed = pre * inv
    dnorm = cotangent[0].astype(jnp.float32) * gain
    dpre = (inv * (dnorm - normed * jnp.mean(dnorm * normed, axis=1, keepdims=True))).astype(
        jnp.bfloat16
    )
    part_other = jnp.einsum(
        "tzyi,to->yzio", a_other, dpre, preferred_element_type=jnp.float32
    ).astype(jnp.bfloat16)
    part_own = jnp.einsum(
        "tzyi,to->yzio", a_own, dpre, preferred_element_type=jnp.float32
    ).astype(jnp.bfloat16)
    part = part_own + lax.ppermute(part_other, "core", other)
    part = part.reshape(n_y, n_zh * rows, part.shape[-1])
    part = lax.psum_scatter(part, "y", scatter_dimension=0, tiled=False)
    part = part.reshape(n_zh, rows, part.shape[-1])
    grad = lax.psum_scatter(part, "zh", scatter_dimension=0, tiled=False).astype(jnp.float32)
    stepped = numer[0] - learning_rate * grad
    levels = lax.axis_size("rep").bit_length() - 1

    def pushed(bit):

        def send_pair(pair):
            return jax.tree.map(
                lambda part, own: part.astype(own.dtype),
                from_partner(shortened(pair), "rep", bit),
                pair,
            )

        return send_pair

    other_numer, other_weight = lax.switch(
        round_bit[0], [pushed(level) for level in range(levels)], (stepped, pweight)
    )
    new_numer = (0.5 * (stepped + other_numer))[None]
    new_pweight = 0.5 * (pweight + other_weight)
    return (new_numer, new_pweight)


def solution(mesh):
    n_rep, n_shard = mesh.devices.shape
    devices = np.asarray(mesh.devices).reshape(n_rep, 2, n_shard // 4, 2)
    split = Mesh(devices, ("rep", "zh", "y", "core"))
    rows = P("rep", ("zh", "y", "core"), None)
    in_specs = (rows, rows, rows, P(), rows, P("rep"), P())
    out_specs = (rows, P("rep"))
    return jax.shard_map(
        on_device, mesh=split, in_specs=in_specs, out_specs=out_specs, check_vma=False
    )
```

```python
import jax
import jax.numpy as jnp
import numpy as np
from jax import lax
from jax.sharding import Mesh, PartitionSpec as P

EPS = 1e-05
learning_rate = 0.5


def shortened(shard):

    def short(part):
        return part.astype(jnp.bfloat16) if part.dtype == jnp.float32 else part

    return jax.tree.map(short, shard)


def from_partner(shard, axis, apart):
    return lax.ppermute(shard, axis, [(i, i ^ 1 << apart) for i in range(lax.axis_size(axis))])


def on_device(attn, resid, cotangent, gain, numer, pweight, round_bit):
    n_zh = lax.axis_size("zh")
    n_y = lax.axis_size("y")
    n_core = lax.axis_size("core")
    acts = attn[0]
    tok, din = acts.shape
    rows = din // (n_zh * n_y * n_core)
    weight_rows = (numer[0] / pweight[0]).astype(jnp.bfloat16)
    me_c = lax.axis_index("core")
    me_z = lax.axis_index("zh")
    swap_core = [(i, i ^ 1) for i in range(n_core)]
    swap_z = [(i, i ^ 1) for i in range(n_zh)]
    acts5 = acts.reshape(tok, n_zh, n_y, n_core, rows)

    def cols(z, c):
        near = lax.dynamic_index_in_dim(acts5, z, axis=1, keepdims=False)
        return lax.dynamic_index_in_dim(near, c, axis=2, keepdims=False)

    w_near = lax.all_gather(weight_rows, "y", axis=0, tiled=False)
    w_near, w_cross = lax.optimization_barrier((w_near, lax.ppermute(weight_rows, "zh", swap_z)))
    w_far = lax.all_gather(w_cross, "y", axis=0, tiled=False)
    w_near_o = lax.ppermute(w_near, "core", swap_core)
    w_far_o = lax.ppermute(w_far, "core", swap_core)

    def mm(a, w):
        return jnp.einsum("tyi,yio->to", a, w, preferred_element_type=jnp.float32)

    pre = (
        resid[0].astype(jnp.float32)
        + mm(cols(me_z, me_c), w_near)
        + mm(cols(me_z, 1 - me_c), w_near_o)
        + mm(cols(1 - me_z, me_c), w_far)
        + mm(cols(1 - me_z, 1 - me_c), w_far_o)
    )
    inv = lax.rsqrt(jnp.mean(pre * pre, axis=1, keepdims=True) + EPS)
    normed = pre * inv
    dnorm = cotangent[0].astype(jnp.float32) * gain
    dpre = (inv * (dnorm - normed * jnp.mean(dnorm * normed, axis=1, keepdims=True))).astype(
        jnp.bfloat16
    )

    def tm(a):
        return jnp.einsum("tyi,to->yio", a, dpre, preferred_element_type=jnp.float32).astype(
            jnp.bfloat16
        )

    far = tm(cols(1 - me_z, me_c)) + lax.ppermute(tm(cols(1 - me_z, 1 - me_c)), "core", swap_core)
    far = lax.ppermute(lax.psum_scatter(far, "y", scatter_dimension=0, tiled=False), "zh", swap_z)
    near = tm(cols(me_z, me_c)) + lax.ppermute(tm(cols(me_z, 1 - me_c)), "core", swap_core)
    near = lax.psum_scatter(near, "y", scatter_dimension=0, tiled=False)
    grad = near.astype(jnp.float32) + far.astype(jnp.float32)
    stepped = numer[0] - learning_rate * grad
    levels = lax.axis_size("rep").bit_length() - 1

    def pushed(bit):

        def send_pair(pair):
            return jax.tree.map(
                lambda part, own: part.astype(own.dtype),
                from_partner(shortened(pair), "rep", bit),
                pair,
            )

        return send_pair

    other_numer, other_weight = lax.switch(
        round_bit[0], [pushed(level) for level in range(levels)], (stepped, pweight)
    )
    new_numer = (0.5 * (stepped + other_numer))[None]
    new_pweight = 0.5 * (pweight + other_weight)
    return (new_numer, new_pweight)


def solution(mesh):
    n_rep, n_shard = mesh.devices.shape
    devices = np.asarray(mesh.devices).reshape(n_rep, 2, n_shard // 4, 2)
    split = Mesh(devices, ("rep", "zh", "y", "core"))
    rows = P("rep", ("zh", "y", "core"), None)
    in_specs = (rows, rows, rows, P(), rows, P("rep"), P())
    out_specs = (rows, P("rep"))
    return jax.shard_map(
        on_device, mesh=split, in_specs=in_specs, out_specs=out_specs, check_vma=False
    )
```

```python
import jax
import jax.numpy as jnp
import numpy as np
from jax import lax
from jax.sharding import Mesh, PartitionSpec as P

EPS = 1e-05
learning_rate = 0.5


def shortened(shard):

    def short(part):
        return part.astype(jnp.bfloat16) if part.dtype == jnp.float32 else part

    return jax.tree.map(short, shard)


def from_partner(shard, axis, apart):
    return lax.ppermute(shard, axis, [(i, i ^ 1 << apart) for i in range(lax.axis_size(axis))])


def on_device(attn, resid, cotangent, gain, numer, pweight, round_bit):
    n_zh = lax.axis_size("zh")
    n_y = lax.axis_size("y")
    n_core = lax.axis_size("core")
    acts = attn[0]
    tok, din = acts.shape
    rows = din // (n_zh * n_y * n_core)
    weight_rows = (numer[0] / pweight[0]).astype(jnp.bfloat16)
    me_c = lax.axis_index("core")
    me_z = lax.axis_index("zh")
    swap_core = [(i, i ^ 1) for i in range(n_core)]
    swap_z = [(i, i ^ 1) for i in range(n_zh)]
    acts5 = acts.reshape(tok, n_zh, n_y, n_core, rows)

    def cols(z, c):
        near = lax.dynamic_index_in_dim(acts5, z, axis=1, keepdims=False)
        return lax.dynamic_index_in_dim(near, c, axis=2, keepdims=False)

    w_near = lax.all_gather(weight_rows, "y", axis=0, tiled=False)
    a_nn, a_no = cols(me_z, me_c), cols(me_z, 1 - me_c)
    a_fn, a_fo = cols(1 - me_z, me_c), cols(1 - me_z, 1 - me_c)
    w_near, w_cross, a_nn, a_no, a_fn, a_fo = lax.optimization_barrier(
        (w_near, lax.ppermute(weight_rows, "zh", swap_z), a_nn, a_no, a_fn, a_fo)
    )
    w_far = lax.all_gather(w_cross, "y", axis=0, tiled=False)
    w_near_o = lax.ppermute(w_near, "core", swap_core)
    w_far_o = lax.ppermute(w_far, "core", swap_core)

    def mm(a, w):
        return jnp.einsum("tyi,yio->to", a, w, preferred_element_type=jnp.float32)

    pre_near = resid[0].astype(jnp.float32) + mm(a_nn, w_near)
    pre_near = pre_near + mm(a_no, w_near_o)
    pre = pre_near + mm(a_fn, w_far) + mm(a_fo, w_far_o)
    inv = lax.rsqrt(jnp.mean(pre * pre, axis=1, keepdims=True) + EPS)
    normed = pre * inv
    dnorm = cotangent[0].astype(jnp.float32) * gain
    dpre = (inv * (dnorm - normed * jnp.mean(dnorm * normed, axis=1, keepdims=True))).astype(
        jnp.bfloat16
    )

    def tm(a):
        return jnp.einsum("tyi,to->yio", a, dpre, preferred_element_type=jnp.float32).astype(
            jnp.bfloat16
        )

    def own_plus_other(a_own, a_other):
        sent = lax.ppermute(tm(a_other), "core", swap_core)
        (own,) = lax.optimization_barrier((tm(a_own),))
        return own + sent

    far = own_plus_other(a_fn, a_fo)
    far = lax.ppermute(lax.psum_scatter(far, "y", scatter_dimension=0, tiled=False), "zh", swap_z)
    near = own_plus_other(a_nn, a_no)
    near = lax.psum_scatter(near, "y", scatter_dimension=0, tiled=False)
    grad = near.astype(jnp.float32) + far.astype(jnp.float32)
    stepped = numer[0] - learning_rate * grad
    levels = lax.axis_size("rep").bit_length() - 1

    def pushed(bit):

        def send(part):
            return from_partner(shortened(part), "rep", bit).astype(part.dtype)

        return send

    def gossip(part):
        return lax.switch(round_bit[0], [pushed(level) for level in range(levels)], part)

    new_pweight = 0.5 * (pweight + gossip(pweight))
    new_numer = (0.5 * (stepped + gossip(stepped)))[None]
    return (new_numer, new_pweight)


def solution(mesh):
    n_rep, n_shard = mesh.devices.shape
    devices = np.asarray(mesh.devices).reshape(n_rep, 2, n_shard // 4, 2)
    split = Mesh(devices, ("rep", "zh", "y", "core"))
    rows = P("rep", ("zh", "y", "core"), None)
    in_specs = (rows, rows, rows, P(), rows, P("rep"), P())
    out_specs = (rows, P("rep"))
    return jax.shard_map(
        on_device, mesh=split, in_specs=in_specs, out_specs=out_specs, check_vma=False
    )
```

```python
import jax
import jax.numpy as jnp
import numpy as np
from jax import lax
from jax.sharding import Mesh, PartitionSpec as P

EPS = 1e-05
learning_rate = 0.5


def shortened(shard):

    def short(part):
        return part.astype(jnp.bfloat16) if part.dtype == jnp.float32 else part

    return jax.tree.map(short, shard)


def from_partner(shard, axis, apart):
    return lax.ppermute(shard, axis, [(i, i ^ 1 << apart) for i in range(lax.axis_size(axis))])


def ring_gather(piece, axis):
    n = lax.axis_size(axis)
    assert n == 4
    cw = [(i, (i + 1) % n) for i in range(n)]
    ccw = [(i, (i - 1) % n) for i in range(n)]
    half = piece.shape[0] // 2
    left = lax.ppermute(piece, axis, cw)
    right = lax.ppermute(piece, axis, ccw)
    opposite = jnp.concatenate(
        [lax.ppermute(left[:half], axis, cw), lax.ppermute(right[half:], axis, ccw)], axis=0
    )
    return jnp.stack([piece, right, opposite, left])


def ring_reduce(parts, axis):
    n = lax.axis_size(axis)
    assert n == 4
    cw = [(i, (i + 1) % n) for i in range(n)]
    ccw = [(i, (i - 1) % n) for i in range(n)]
    half = parts.shape[1] // 2
    f32 = parts.astype(jnp.float32)
    got_a = lax.ppermute(parts[2, :half], axis, cw).astype(jnp.float32)
    got_b = lax.ppermute(parts[2, half:], axis, ccw).astype(jnp.float32)
    to_next = jnp.concatenate([f32[1, :half] + got_a, f32[1, half:]], axis=0)
    to_prev = jnp.concatenate([f32[3, :half], f32[3, half:] + got_b], axis=0)
    from_prev = lax.ppermute(to_next.astype(jnp.bfloat16), axis, cw).astype(jnp.float32)
    from_next = lax.ppermute(to_prev.astype(jnp.bfloat16), axis, ccw).astype(jnp.float32)
    return f32[0] + from_prev + from_next


def on_device(attn, resid, cotangent, gain, numer, pweight, round_bit):
    n_zh = lax.axis_size("zh")
    n_y = lax.axis_size("y")
    n_core = lax.axis_size("core")
    acts = attn[0]
    tok, din = acts.shape
    rows = din // (n_zh * n_y * n_core)
    weight_rows = (numer[0] / pweight[0]).astype(jnp.bfloat16)
    me_c = lax.axis_index("core")
    me_z = lax.axis_index("zh")
    swap_core = [(i, i ^ 1) for i in range(n_core)]
    swap_z = [(i, i ^ 1) for i in range(n_zh)]
    acts5 = acts.reshape(tok, n_zh, n_y, n_core, rows)

    def cols(z, c):
        near = lax.dynamic_index_in_dim(acts5, z, axis=1, keepdims=False)
        return lax.dynamic_index_in_dim(near, c, axis=2, keepdims=False)

    w_near = lax.all_gather(weight_rows, "y", axis=0, tiled=False)
    a_nn, a_no = cols(me_z, me_c), cols(me_z, 1 - me_c)
    me_y = lax.axis_index("y")
    a_fn = jnp.roll(cols(1 - me_z, me_c), -me_y, axis=1)
    a_fo = jnp.roll(cols(1 - me_z, 1 - me_c), -me_y, axis=1)
    w_near, w_cross, a_nn, a_no, a_fn, a_fo = lax.optimization_barrier(
        (w_near, lax.ppermute(weight_rows, "zh", swap_z), a_nn, a_no, a_fn, a_fo)
    )
    w_far = ring_gather(w_cross, "y")
    w_near_o = lax.ppermute(w_near, "core", swap_core)
    w_far_o = lax.ppermute(w_far, "core", swap_core)

    def mm(a, w):
        return jnp.einsum("tyi,yio->to", a, w, preferred_element_type=jnp.float32)

    pre_near = resid[0].astype(jnp.float32) + mm(a_nn, w_near)
    pre_near = pre_near + mm(a_no, w_near_o)
    pre = pre_near + mm(a_fn, w_far) + mm(a_fo, w_far_o)
    inv = lax.rsqrt(jnp.mean(pre * pre, axis=1, keepdims=True) + EPS)
    normed = pre * inv
    dnorm = cotangent[0].astype(jnp.float32) * gain
    dpre = (inv * (dnorm - normed * jnp.mean(dnorm * normed, axis=1, keepdims=True))).astype(
        jnp.bfloat16
    )

    def tm(a):
        return jnp.einsum("tyi,to->yio", a, dpre, preferred_element_type=jnp.float32).astype(
            jnp.bfloat16
        )

    def own_plus_other(a_own, a_other):
        sent = lax.ppermute(tm(a_other), "core", swap_core)
        (own,) = lax.optimization_barrier((tm(a_own),))
        return own + sent

    far = own_plus_other(a_fn, a_fo)
    far = lax.ppermute(ring_reduce(far, "y").astype(jnp.bfloat16), "zh", swap_z)
    near = own_plus_other(a_nn, a_no)
    near = lax.psum_scatter(near, "y", scatter_dimension=0, tiled=False)
    grad = near.astype(jnp.float32) + far.astype(jnp.float32)
    stepped = numer[0] - learning_rate * grad
    levels = lax.axis_size("rep").bit_length() - 1

    def pushed(bit):

        def send(part):
            return from_partner(shortened(part), "rep", bit).astype(part.dtype)

        return send

    def gossip(part):
        return lax.switch(round_bit[0], [pushed(level) for level in range(levels)], part)

    new_pweight = 0.5 * (pweight + gossip(pweight))
    new_numer = (0.5 * (stepped + gossip(stepped)))[None]
    return (new_numer, new_pweight)


def solution(mesh):
    n_rep, n_shard = mesh.devices.shape
    devices = np.asarray(mesh.devices).reshape(n_rep, 2, n_shard // 4, 2)
    split = Mesh(devices, ("rep", "zh", "y", "core"))
    rows = P("rep", ("zh", "y", "core"), None)
    in_specs = (rows, rows, rows, P(), rows, P("rep"), P())
    out_specs = (rows, P("rep"))
    return jax.shard_map(
        on_device, mesh=split, in_specs=in_specs, out_specs=out_specs, check_vma=False
    )
```

```python
import jax
import jax.numpy as jnp
import numpy as np
from jax import lax
from jax.sharding import Mesh, PartitionSpec as P

EPS = 1e-05
learning_rate = 0.5


def shortened(shard):

    def short(part):
        return part.astype(jnp.bfloat16) if part.dtype == jnp.float32 else part

    return jax.tree.map(short, shard)


def from_partner(shard, axis, apart):
    return lax.ppermute(shard, axis, [(i, i ^ 1 << apart) for i in range(lax.axis_size(axis))])


def ring_gather(piece, axis):
    n = lax.axis_size(axis)
    assert n == 4
    cw = [(i, (i + 1) % n) for i in range(n)]
    ccw = [(i, (i - 1) % n) for i in range(n)]
    half = piece.shape[0] // 2
    left = lax.ppermute(piece, axis, cw)
    right = lax.ppermute(piece, axis, ccw)
    opposite = jnp.concatenate(
        [lax.ppermute(left[:half], axis, cw), lax.ppermute(right[half:], axis, ccw)], axis=0
    )
    return jnp.stack([piece, right, opposite, left])


def ring_reduce(parts, axis):
    n = lax.axis_size(axis)
    assert n == 4
    cw = [(i, (i + 1) % n) for i in range(n)]
    ccw = [(i, (i - 1) % n) for i in range(n)]
    half = parts.shape[1] // 2
    f32 = parts.astype(jnp.float32)
    got_a = lax.ppermute(parts[2, :half], axis, cw).astype(jnp.float32)
    got_b = lax.ppermute(parts[2, half:], axis, ccw).astype(jnp.float32)
    to_next = jnp.concatenate([f32[1, :half] + got_a, f32[1, half:]], axis=0)
    to_prev = jnp.concatenate([f32[3, :half], f32[3, half:] + got_b], axis=0)
    from_prev = lax.ppermute(to_next.astype(jnp.bfloat16), axis, cw).astype(jnp.float32)
    from_next = lax.ppermute(to_prev.astype(jnp.bfloat16), axis, ccw).astype(jnp.float32)
    return f32[0] + from_prev + from_next


def on_device(attn, resid, cotangent, gain, numer, pweight, round_bit):
    n_zh = lax.axis_size("zh")
    n_y = lax.axis_size("y")
    n_core = lax.axis_size("core")
    acts = attn[0]
    tok, din = acts.shape
    rows = din // (n_zh * n_y * n_core)
    weight_rows = (numer[0] / pweight[0]).astype(jnp.bfloat16)
    me_c = lax.axis_index("core")
    me_z = lax.axis_index("zh")
    swap_core = [(i, i ^ 1) for i in range(n_core)]
    swap_z = [(i, i ^ 1) for i in range(n_zh)]
    acts5 = acts.reshape(tok, n_zh, n_y, n_core, rows)

    def cols(z, c):
        near = lax.dynamic_index_in_dim(acts5, z, axis=1, keepdims=False)
        return lax.dynamic_index_in_dim(near, c, axis=2, keepdims=False)

    w_near = lax.all_gather(weight_rows, "y", axis=0, tiled=False)
    a_nn, a_no = cols(me_z, me_c), cols(me_z, 1 - me_c)
    me_y = lax.axis_index("y")
    a_fn = jnp.roll(cols(1 - me_z, me_c), -me_y, axis=1)
    a_fo = jnp.roll(cols(1 - me_z, 1 - me_c), -me_y, axis=1)
    w_near, w_cross, a_nn, a_no, a_fn, a_fo = lax.optimization_barrier(
        (w_near, lax.ppermute(weight_rows, "zh", swap_z), a_nn, a_no, a_fn, a_fo)
    )
    w_far = ring_gather(w_cross, "y")
    w_near_o = lax.ppermute(w_near, "core", swap_core)
    w_far_o = lax.ppermute(w_far, "core", swap_core)

    def mm(a, w):
        return jnp.einsum("tyi,yio->to", a, w, preferred_element_type=jnp.float32)

    pre_near = resid[0].astype(jnp.float32) + mm(a_nn, w_near)
    pre_near = pre_near + mm(a_no, w_near_o)
    pre = pre_near + mm(a_fn, w_far) + mm(a_fo, w_far_o)
    inv = lax.rsqrt(jnp.mean(pre * pre, axis=1, keepdims=True) + EPS)
    normed = pre * inv
    dnorm = cotangent[0].astype(jnp.float32) * gain
    dpre = (inv * (dnorm - normed * jnp.mean(dnorm * normed, axis=1, keepdims=True))).astype(
        jnp.bfloat16
    )

    def tm(a):
        return jnp.einsum("tyi,to->yio", a, dpre, preferred_element_type=jnp.float32).astype(
            jnp.bfloat16
        )

    def own_plus_other(a_own, a_other):
        sent = lax.ppermute(tm(a_other), "core", swap_core)
        (own,) = lax.optimization_barrier((tm(a_own),))
        return own + sent

    far = own_plus_other(a_fn, a_fo)
    far = ring_reduce(far, "y").astype(jnp.bfloat16)
    near = own_plus_other(a_nn, a_no)
    near, far = lax.optimization_barrier((near, far))
    far = lax.ppermute(far, "zh", swap_z)
    near = lax.psum_scatter(near, "y", scatter_dimension=0, tiled=False)
    grad = near.astype(jnp.float32) + far.astype(jnp.float32)
    stepped = numer[0] - learning_rate * grad
    levels = lax.axis_size("rep").bit_length() - 1

    def pushed(bit):

        def send(part):
            return from_partner(shortened(part), "rep", bit).astype(part.dtype)

        return send

    def gossip(part):
        return lax.switch(round_bit[0], [pushed(level) for level in range(levels)], part)

    new_pweight = 0.5 * (pweight + gossip(pweight))
    new_numer = (0.5 * (stepped + gossip(stepped)))[None]
    return (new_numer, new_pweight)


def solution(mesh):
    n_rep, n_shard = mesh.devices.shape
    devices = np.asarray(mesh.devices).reshape(n_rep, 2, n_shard // 4, 2)
    split = Mesh(devices, ("rep", "zh", "y", "core"))
    rows = P("rep", ("zh", "y", "core"), None)
    in_specs = (rows, rows, rows, P(), rows, P("rep"), P())
    out_specs = (rows, P("rep"))
    return jax.shard_map(
        on_device, mesh=split, in_specs=in_specs, out_specs=out_specs, check_vma=False
    )
```

```python
import jax
import jax.numpy as jnp
import numpy as np
from jax import lax
from jax.sharding import Mesh, PartitionSpec as P

EPS = 1e-05
learning_rate = 0.5


def shortened(shard):

    def short(part):
        return part.astype(jnp.bfloat16) if part.dtype == jnp.float32 else part

    return jax.tree.map(short, shard)


def from_partner(shard, axis, apart):
    return lax.ppermute(shard, axis, [(i, i ^ 1 << apart) for i in range(lax.axis_size(axis))])


def ring_gather(piece, axis, during):
    n = lax.axis_size(axis)
    assert n == 4
    cw = [(i, (i + 1) % n) for i in range(n)]
    ccw = [(i, (i - 1) % n) for i in range(n)]
    half = piece.shape[0] // 2
    left = lax.ppermute(piece, axis, cw)
    right = lax.ppermute(piece, axis, ccw)
    left, right, held = lax.optimization_barrier((left, right, during()))
    opposite = jnp.concatenate(
        [lax.ppermute(left[:half], axis, cw), lax.ppermute(right[half:], axis, ccw)], axis=0
    )
    return jnp.stack([piece, right, opposite, left]), held


def ring_reduce(parts, axis):
    n = lax.axis_size(axis)
    assert n == 4
    cw = [(i, (i + 1) % n) for i in range(n)]
    ccw = [(i, (i - 1) % n) for i in range(n)]
    half = parts.shape[1] // 2
    f32 = parts.astype(jnp.float32)
    got_a = lax.ppermute(parts[2, :half], axis, cw).astype(jnp.float32)
    got_b = lax.ppermute(parts[2, half:], axis, ccw).astype(jnp.float32)
    to_next = jnp.concatenate([f32[1, :half] + got_a, f32[1, half:]], axis=0)
    to_prev = jnp.concatenate([f32[3, :half], f32[3, half:] + got_b], axis=0)
    from_prev = lax.ppermute(to_next.astype(jnp.bfloat16), axis, cw).astype(jnp.float32)
    from_next = lax.ppermute(to_prev.astype(jnp.bfloat16), axis, ccw).astype(jnp.float32)
    return f32[0] + from_prev + from_next


def on_device(attn, resid, cotangent, gain, numer, pweight, round_bit):
    n_zh = lax.axis_size("zh")
    n_y = lax.axis_size("y")
    n_core = lax.axis_size("core")
    acts = attn[0]
    tok, din = acts.shape
    rows = din // (n_zh * n_y * n_core)
    weight_rows = (numer[0] / pweight[0]).astype(jnp.bfloat16)
    me_c = lax.axis_index("core")
    me_z = lax.axis_index("zh")
    swap_core = [(i, i ^ 1) for i in range(n_core)]
    swap_z = [(i, i ^ 1) for i in range(n_zh)]
    acts5 = acts.reshape(tok, n_zh, n_y, n_core, rows)

    def cols(z, c):
        near = lax.dynamic_index_in_dim(acts5, z, axis=1, keepdims=False)
        return lax.dynamic_index_in_dim(near, c, axis=2, keepdims=False)

    w_near = lax.all_gather(weight_rows, "y", axis=0, tiled=False)
    a_nn, a_no = cols(me_z, me_c), cols(me_z, 1 - me_c)
    me_y = lax.axis_index("y")
    a_fn = jnp.roll(cols(1 - me_z, me_c), -me_y, axis=1)
    a_fo = jnp.roll(cols(1 - me_z, 1 - me_c), -me_y, axis=1)
    w_near, w_cross, a_nn, a_no, a_fn, a_fo = lax.optimization_barrier(
        (w_near, lax.ppermute(weight_rows, "zh", swap_z), a_nn, a_no, a_fn, a_fo)
    )
    w_near_o = lax.ppermute(w_near, "core", swap_core)

    def mm(a, w):
        return jnp.einsum("tyi,yio->to", a, w, preferred_element_type=jnp.float32)

    def near_products():
        pre_near = resid[0].astype(jnp.float32) + mm(a_nn, w_near)
        return pre_near + mm(a_no, w_near_o)

    w_far, pre_near = ring_gather(w_cross, "y", near_products)
    w_far_o = lax.ppermute(w_far, "core", swap_core)
    pre = pre_near + mm(a_fn, w_far) + mm(a_fo, w_far_o)
    inv = lax.rsqrt(jnp.mean(pre * pre, axis=1, keepdims=True) + EPS)
    normed = pre * inv
    dnorm = cotangent[0].astype(jnp.float32) * gain
    dpre = (inv * (dnorm - normed * jnp.mean(dnorm * normed, axis=1, keepdims=True))).astype(
        jnp.bfloat16
    )

    def tm(a):
        return jnp.einsum("tyi,to->yio", a, dpre, preferred_element_type=jnp.float32).astype(
            jnp.bfloat16
        )

    def own_plus_other(a_own, a_other):
        sent = lax.ppermute(tm(a_other), "core", swap_core)
        (own,) = lax.optimization_barrier((tm(a_own),))
        return own + sent

    far = own_plus_other(a_fn, a_fo)
    far = ring_reduce(far, "y").astype(jnp.bfloat16)
    near = own_plus_other(a_nn, a_no)
    near, far = lax.optimization_barrier((near, far))
    far = lax.ppermute(far, "zh", swap_z)
    near = lax.psum_scatter(near, "y", scatter_dimension=0, tiled=False)
    grad = near.astype(jnp.float32) + far.astype(jnp.float32)
    stepped = numer[0] - learning_rate * grad
    levels = lax.axis_size("rep").bit_length() - 1

    def pushed(bit):

        def send(part):
            return from_partner(shortened(part), "rep", bit).astype(part.dtype)

        return send

    def gossip(part):
        return lax.switch(round_bit[0], [pushed(level) for level in range(levels)], part)

    new_pweight = 0.5 * (pweight + gossip(pweight))
    new_numer = (0.5 * (stepped + gossip(stepped)))[None]
    return (new_numer, new_pweight)


def solution(mesh):
    n_rep, n_shard = mesh.devices.shape
    devices = np.asarray(mesh.devices).reshape(n_rep, 2, n_shard // 4, 2)
    split = Mesh(devices, ("rep", "zh", "y", "core"))
    rows = P("rep", ("zh", "y", "core"), None)
    in_specs = (rows, rows, rows, P(), rows, P("rep"), P())
    out_specs = (rows, P("rep"))
    return jax.shard_map(
        on_device, mesh=split, in_specs=in_specs, out_specs=out_specs, check_vma=False
    )
```

```python
import jax
import jax.numpy as jnp
import numpy as np
from jax import lax
from jax.sharding import Mesh, PartitionSpec as P

EPS = 1e-05
learning_rate = 0.5


def shortened(shard):

    def short(part):
        return part.astype(jnp.bfloat16) if part.dtype == jnp.float32 else part

    return jax.tree.map(short, shard)


def from_partner(shard, axis, apart):
    return lax.ppermute(shard, axis, [(i, i ^ 1 << apart) for i in range(lax.axis_size(axis))])


def ring_gather(piece, axis, during):
    n = lax.axis_size(axis)
    assert n == 4
    cw = [(i, (i + 1) % n) for i in range(n)]
    ccw = [(i, (i - 1) % n) for i in range(n)]
    half = piece.shape[0] // 2
    left = lax.ppermute(piece, axis, cw)
    right = lax.ppermute(piece, axis, ccw)
    left, right, held = lax.optimization_barrier((left, right, during()))
    opposite = jnp.concatenate(
        [lax.ppermute(left[:half], axis, cw), lax.ppermute(right[half:], axis, ccw)], axis=0
    )
    return jnp.stack([piece, right, opposite, left]), held


def ring_reduce(parts, axis):
    n = lax.axis_size(axis)
    assert n == 4
    cw = [(i, (i + 1) % n) for i in range(n)]
    ccw = [(i, (i - 1) % n) for i in range(n)]
    half = parts.shape[1] // 2
    f32 = parts.astype(jnp.float32)
    got_a = lax.ppermute(parts[2, :half], axis, cw).astype(jnp.float32)
    got_b = lax.ppermute(parts[2, half:], axis, ccw).astype(jnp.float32)
    to_next = jnp.concatenate([f32[1, :half] + got_a, f32[1, half:]], axis=0)
    to_prev = jnp.concatenate([f32[3, :half], f32[3, half:] + got_b], axis=0)
    from_prev = lax.ppermute(to_next.astype(jnp.bfloat16), axis, cw).astype(jnp.float32)
    from_next = lax.ppermute(to_prev.astype(jnp.bfloat16), axis, ccw).astype(jnp.float32)
    return f32[0] + from_prev + from_next


def on_device(attn, resid, cotangent, gain, numer, pweight, round_bit):
    n_zh = lax.axis_size("zh")
    n_y = lax.axis_size("y")
    n_core = lax.axis_size("core")
    acts = attn[0]
    tok, din = acts.shape
    rows = din // (n_zh * n_y * n_core)
    weight_rows = (numer[0] / pweight[0]).astype(jnp.bfloat16)
    me_c = lax.axis_index("core")
    me_z = lax.axis_index("zh")
    swap_core = [(i, i ^ 1) for i in range(n_core)]
    swap_z = [(i, i ^ 1) for i in range(n_zh)]
    acts5 = acts.reshape(tok, n_zh, n_y, n_core, rows)

    def cols(z, c):
        near = lax.dynamic_index_in_dim(acts5, z, axis=1, keepdims=False)
        return lax.dynamic_index_in_dim(near, c, axis=2, keepdims=False)

    w_near = lax.all_gather(weight_rows, "y", axis=0, tiled=False)
    a_nn, a_no = cols(me_z, me_c), cols(me_z, 1 - me_c)
    me_y = lax.axis_index("y")
    a_fn = jnp.roll(cols(1 - me_z, me_c), -me_y, axis=1)
    a_fo = jnp.roll(cols(1 - me_z, 1 - me_c), -me_y, axis=1)
    w_near, w_cross, a_nn, a_no, a_fn, a_fo = lax.optimization_barrier(
        (w_near, lax.ppermute(weight_rows, "zh", swap_z), a_nn, a_no, a_fn, a_fo)
    )
    w_near_o = lax.ppermute(w_near, "core", swap_core)

    def mm(a, w):
        return jnp.einsum("tyi,yio->to", a, w, preferred_element_type=jnp.float32)

    def near_products():
        pre_near = resid[0].astype(jnp.float32) + mm(a_nn, w_near)
        return pre_near + mm(a_no, w_near_o)

    w_far, pre_near = ring_gather(w_cross, "y", near_products)
    w_far_o = lax.ppermute(w_far, "core", swap_core)
    pre = pre_near + mm(a_fn, w_far) + mm(a_fo, w_far_o)
    inv = lax.rsqrt(jnp.mean(pre * pre, axis=1, keepdims=True) + EPS)
    normed = pre * inv
    dnorm = cotangent[0].astype(jnp.float32) * gain
    dpre = (inv * (dnorm - normed * jnp.mean(dnorm * normed, axis=1, keepdims=True))).astype(
        jnp.bfloat16
    )

    def tm(a):
        return jnp.einsum("tyi,to->yio", a, dpre, preferred_element_type=jnp.float32).astype(
            jnp.bfloat16
        )

    def own_plus_other(a_own, a_other):
        sent = lax.ppermute(tm(a_other), "core", swap_core)
        (own,) = lax.optimization_barrier((tm(a_own),))
        return own + sent

    far = own_plus_other(a_fn, a_fo)
    far = ring_reduce(far, "y").astype(jnp.bfloat16)
    near = own_plus_other(jnp.roll(a_nn, -me_y, axis=1), jnp.roll(a_no, -me_y, axis=1))
    near, far = lax.optimization_barrier((near, far))
    far = lax.ppermute(far, "zh", swap_z)
    near = ring_reduce(near, "y")
    grad = near.astype(jnp.float32) + far.astype(jnp.float32)
    stepped = numer[0] - learning_rate * grad
    levels = lax.axis_size("rep").bit_length() - 1

    def pushed(bit):

        def send(part):
            return from_partner(shortened(part), "rep", bit).astype(part.dtype)

        return send

    def gossip(part):
        return lax.switch(round_bit[0], [pushed(level) for level in range(levels)], part)

    new_pweight = 0.5 * (pweight + gossip(pweight))
    new_numer = (0.5 * (stepped + gossip(stepped)))[None]
    return (new_numer, new_pweight)


def solution(mesh):
    n_rep, n_shard = mesh.devices.shape
    devices = np.asarray(mesh.devices).reshape(n_rep, 2, n_shard // 4, 2)
    split = Mesh(devices, ("rep", "zh", "y", "core"))
    rows = P("rep", ("zh", "y", "core"), None)
    in_specs = (rows, rows, rows, P(), rows, P("rep"), P())
    out_specs = (rows, P("rep"))
    return jax.shard_map(
        on_device, mesh=split, in_specs=in_specs, out_specs=out_specs, check_vma=False
    )
```

```python
import jax
import jax.numpy as jnp
import numpy as np
from jax import lax
from jax.sharding import Mesh, PartitionSpec as P

EPS = 1e-05
learning_rate = 0.5


def shortened(shard):

    def short(part):
        return part.astype(jnp.bfloat16) if part.dtype == jnp.float32 else part

    return jax.tree.map(short, shard)


def from_partner(shard, axis, apart):
    return lax.ppermute(shard, axis, [(i, i ^ 1 << apart) for i in range(lax.axis_size(axis))])


def ring_gather(piece, axis, during):
    n = lax.axis_size(axis)
    assert n == 4
    cw = [(i, (i + 1) % n) for i in range(n)]
    ccw = [(i, (i - 1) % n) for i in range(n)]
    half = piece.shape[0] // 2
    left = lax.ppermute(piece, axis, cw)
    right = lax.ppermute(piece, axis, ccw)
    left, right, held = lax.optimization_barrier((left, right, during()))
    opposite = jnp.concatenate(
        [lax.ppermute(left[:half], axis, cw), lax.ppermute(right[half:], axis, ccw)], axis=0
    )
    return [piece, right, opposite, left], held


def ring_reduce(parts, axis):
    n = lax.axis_size(axis)
    assert n == 4
    cw = [(i, (i + 1) % n) for i in range(n)]
    ccw = [(i, (i - 1) % n) for i in range(n)]
    half = parts.shape[1] // 2
    f32 = parts.astype(jnp.float32)
    got_a = lax.ppermute(parts[2, :half], axis, cw).astype(jnp.float32)
    got_b = lax.ppermute(parts[2, half:], axis, ccw).astype(jnp.float32)
    to_next = jnp.concatenate([f32[1, :half] + got_a, f32[1, half:]], axis=0)
    to_prev = jnp.concatenate([f32[3, :half], f32[3, half:] + got_b], axis=0)
    from_prev = lax.ppermute(to_next.astype(jnp.bfloat16), axis, cw).astype(jnp.float32)
    from_next = lax.ppermute(to_prev.astype(jnp.bfloat16), axis, ccw).astype(jnp.float32)
    return f32[0] + from_prev + from_next


def on_device(attn, resid, cotangent, gain, numer, pweight, round_bit):
    n_zh = lax.axis_size("zh")
    n_y = lax.axis_size("y")
    n_core = lax.axis_size("core")
    acts = attn[0]
    tok, din = acts.shape
    rows = din // (n_zh * n_y * n_core)
    weight_rows = (numer[0] / pweight[0]).astype(jnp.bfloat16)
    me_c = lax.axis_index("core")
    me_z = lax.axis_index("zh")
    swap_core = [(i, i ^ 1) for i in range(n_core)]
    swap_z = [(i, i ^ 1) for i in range(n_zh)]
    acts5 = acts.reshape(tok, n_zh, n_y, n_core, rows)

    def cols(z, c):
        near = lax.dynamic_index_in_dim(acts5, z, axis=1, keepdims=False)
        return lax.dynamic_index_in_dim(near, c, axis=2, keepdims=False)

    w_near = lax.all_gather(weight_rows, "y", axis=0, tiled=False)
    a_nn, a_no = cols(me_z, me_c), cols(me_z, 1 - me_c)
    me_y = lax.axis_index("y")
    a_fn = jnp.roll(cols(1 - me_z, me_c), -me_y, axis=1)
    a_fo = jnp.roll(cols(1 - me_z, 1 - me_c), -me_y, axis=1)
    w_near, w_cross, a_nn, a_no, a_fn, a_fo = lax.optimization_barrier(
        (w_near, lax.ppermute(weight_rows, "zh", swap_z), a_nn, a_no, a_fn, a_fo)
    )
    w_near_o = lax.ppermute(w_near, "core", swap_core)

    def mm(a, w):
        return jnp.einsum("tyi,yio->to", a, w, preferred_element_type=jnp.float32)

    def near_products():
        pre_near = resid[0].astype(jnp.float32) + mm(a_nn, w_near)
        return pre_near + mm(a_no, w_near_o)

    pieces, pre_near = ring_gather(w_cross, "y", near_products)
    w_far = jnp.stack(pieces)
    w_far_o = jnp.stack([lax.ppermute(p, "core", swap_core) for p in pieces])
    pre = pre_near + mm(a_fn, w_far) + mm(a_fo, w_far_o)
    inv = lax.rsqrt(jnp.mean(pre * pre, axis=1, keepdims=True) + EPS)
    normed = pre * inv
    dnorm = cotangent[0].astype(jnp.float32) * gain
    dpre = (inv * (dnorm - normed * jnp.mean(dnorm * normed, axis=1, keepdims=True))).astype(
        jnp.bfloat16
    )

    def tm(a):
        return jnp.einsum("tyi,to->yio", a, dpre, preferred_element_type=jnp.float32).astype(
            jnp.bfloat16
        )

    def own_plus_other(a_own, a_other):
        sent = lax.ppermute(tm(a_other), "core", swap_core)
        (own,) = lax.optimization_barrier((tm(a_own),))
        return own + sent

    far = own_plus_other(a_fn, a_fo)
    far = ring_reduce(far, "y").astype(jnp.bfloat16)
    near = own_plus_other(a_nn, a_no)
    near, far = lax.optimization_barrier((near, far))
    far = lax.ppermute(far, "zh", swap_z)
    near = lax.psum_scatter(near, "y", scatter_dimension=0, tiled=False)
    grad = near.astype(jnp.float32) + far.astype(jnp.float32)
    stepped = numer[0] - learning_rate * grad
    levels = lax.axis_size("rep").bit_length() - 1

    def pushed(bit):

        def send(part):
            return from_partner(shortened(part), "rep", bit).astype(part.dtype)

        return send

    def gossip(part):
        return lax.switch(round_bit[0], [pushed(level) for level in range(levels)], part)

    weights = lax.all_gather(pweight, "rep", axis=0, tiled=True)
    partner = lax.axis_index("rep") ^ (1 << round_bit[0])
    new_pweight = 0.5 * (pweight + lax.dynamic_slice_in_dim(weights, partner, 1))
    new_numer = (0.5 * (stepped + gossip(stepped)))[None]
    return (new_numer, new_pweight)


def solution(mesh):
    n_rep, n_shard = mesh.devices.shape
    devices = np.asarray(mesh.devices).reshape(n_rep, 2, n_shard // 4, 2)
    split = Mesh(devices, ("rep", "zh", "y", "core"))
    rows = P("rep", ("zh", "y", "core"), None)
    in_specs = (rows, rows, rows, P(), rows, P("rep"), P())
    out_specs = (rows, P("rep"))
    return jax.shard_map(
        on_device, mesh=split, in_specs=in_specs, out_specs=out_specs, check_vma=False
    )
```

```python
import jax
import jax.numpy as jnp
import numpy as np
from jax import lax
from jax.sharding import Mesh, PartitionSpec as P

EPS = 1e-05
learning_rate = 0.5


def shortened(shard):

    def short(part):
        return part.astype(jnp.bfloat16) if part.dtype == jnp.float32 else part

    return jax.tree.map(short, shard)


def from_partner(shard, axis, apart):
    return lax.ppermute(shard, axis, [(i, i ^ 1 << apart) for i in range(lax.axis_size(axis))])


def ring_gather(piece, axis, during):
    n = lax.axis_size(axis)
    assert n == 4
    cw = [(i, (i + 1) % n) for i in range(n)]
    ccw = [(i, (i - 1) % n) for i in range(n)]
    half = piece.shape[0] // 2
    left = lax.ppermute(piece, axis, cw)
    right = lax.ppermute(piece, axis, ccw)
    left, right, held = lax.optimization_barrier((left, right, during()))
    opposite = jnp.concatenate(
        [lax.ppermute(left[:half], axis, cw), lax.ppermute(right[half:], axis, ccw)], axis=0
    )
    return [piece, right, opposite, left], held


def ring_reduce(parts, axis):
    n = lax.axis_size(axis)
    assert n == 4
    cw = [(i, (i + 1) % n) for i in range(n)]
    ccw = [(i, (i - 1) % n) for i in range(n)]
    half = parts.shape[1] // 2
    f32 = parts.astype(jnp.float32)
    got_a = lax.ppermute(parts[2, :half], axis, cw).astype(jnp.float32)
    got_b = lax.ppermute(parts[2, half:], axis, ccw).astype(jnp.float32)
    to_next = jnp.concatenate([f32[1, :half] + got_a, f32[1, half:]], axis=0)
    to_prev = jnp.concatenate([f32[3, :half], f32[3, half:] + got_b], axis=0)
    from_prev = lax.ppermute(to_next.astype(jnp.bfloat16), axis, cw).astype(jnp.float32)
    from_next = lax.ppermute(to_prev.astype(jnp.bfloat16), axis, ccw).astype(jnp.float32)
    return f32[0] + from_prev + from_next


def on_device(attn, resid, cotangent, gain, numer, pweight, round_bit):
    n_zh = lax.axis_size("zh")
    n_y = lax.axis_size("y")
    n_core = lax.axis_size("core")
    acts = attn[0]
    tok, din = acts.shape
    rows = din // (n_zh * n_y * n_core)
    weight_rows = (numer[0] / pweight[0]).astype(jnp.bfloat16)
    me_c = lax.axis_index("core")
    me_z = lax.axis_index("zh")
    swap_core = [(i, i ^ 1) for i in range(n_core)]
    swap_z = [(i, i ^ 1) for i in range(n_zh)]
    acts5 = acts.reshape(tok, n_zh, n_y, n_core, rows)

    def cols(z, c):
        near = lax.dynamic_index_in_dim(acts5, z, axis=1, keepdims=False)
        return lax.dynamic_index_in_dim(near, c, axis=2, keepdims=False)

    w_near = lax.all_gather(weight_rows, "y", axis=0, tiled=False)
    a_nn, a_no = cols(me_z, me_c), cols(me_z, 1 - me_c)
    me_y = lax.axis_index("y")
    a_fn = jnp.roll(cols(1 - me_z, me_c), -me_y, axis=1)
    a_fo = jnp.roll(cols(1 - me_z, 1 - me_c), -me_y, axis=1)
    w_near, w_cross, a_nn, a_no, a_fn, a_fo = lax.optimization_barrier(
        (w_near, lax.ppermute(weight_rows, "zh", swap_z), a_nn, a_no, a_fn, a_fo)
    )
    w_near_o = lax.ppermute(w_near, "core", swap_core)

    def mm(a, w):
        return jnp.einsum("tyi,yio->to", a, w, preferred_element_type=jnp.float32)

    def near_products():
        pre_near = resid[0].astype(jnp.float32) + mm(a_nn, w_near)
        return pre_near + mm(a_no, w_near_o)

    pieces, pre_near = ring_gather(w_cross, "y", near_products)
    w_far = jnp.stack(pieces)
    piece, right, opposite, left = pieces
    sides = lax.ppermute(jnp.stack([right, left]), "core", swap_core)
    w_far_o = jnp.stack(
        [
            lax.ppermute(piece, "core", swap_core),
            sides[0],
            lax.ppermute(opposite, "core", swap_core),
            sides[1],
        ]
    )
    pre = pre_near + mm(a_fn, w_far) + mm(a_fo, w_far_o)
    inv = lax.rsqrt(jnp.mean(pre * pre, axis=1, keepdims=True) + EPS)
    normed = pre * inv
    dnorm = cotangent[0].astype(jnp.float32) * gain
    dpre = (inv * (dnorm - normed * jnp.mean(dnorm * normed, axis=1, keepdims=True))).astype(
        jnp.bfloat16
    )

    def tm(a):
        return jnp.einsum("tyi,to->yio", a, dpre, preferred_element_type=jnp.float32).astype(
            jnp.bfloat16
        )

    def own_plus_other(a_own, a_other):
        sent = lax.ppermute(tm(a_other), "core", swap_core)
        (own,) = lax.optimization_barrier((tm(a_own),))
        return own + sent

    far = own_plus_other(a_fn, a_fo)
    far = ring_reduce(far, "y").astype(jnp.bfloat16)
    near = own_plus_other(a_nn, a_no)
    near, far = lax.optimization_barrier((near, far))
    far = lax.ppermute(far, "zh", swap_z)
    near = lax.psum_scatter(near, "y", scatter_dimension=0, tiled=False)
    grad = near.astype(jnp.float32) + far.astype(jnp.float32)
    stepped = numer[0] - learning_rate * grad
    levels = lax.axis_size("rep").bit_length() - 1

    def pushed(bit):

        def send(part):
            return from_partner(shortened(part), "rep", bit).astype(part.dtype)

        return send

    def gossip(part):
        return lax.switch(round_bit[0], [pushed(level) for level in range(levels)], part)

    new_pweight = 0.5 * (pweight + gossip(pweight))
    new_numer = (0.5 * (stepped + gossip(stepped)))[None]
    return (new_numer, new_pweight)


def solution(mesh):
    n_rep, n_shard = mesh.devices.shape
    devices = np.asarray(mesh.devices).reshape(n_rep, 2, n_shard // 4, 2)
    split = Mesh(devices, ("rep", "zh", "y", "core"))
    rows = P("rep", ("zh", "y", "core"), None)
    in_specs = (rows, rows, rows, P(), rows, P("rep"), P())
    out_specs = (rows, P("rep"))
    return jax.shard_map(
        on_device, mesh=split, in_specs=in_specs, out_specs=out_specs, check_vma=False
    )
```

```python
import jax
import jax.numpy as jnp
import numpy as np
from jax import lax
from jax.sharding import Mesh, PartitionSpec as P

EPS = 1e-05
learning_rate = 0.5


def shortened(shard):

    def short(part):
        return part.astype(jnp.bfloat16) if part.dtype == jnp.float32 else part

    return jax.tree.map(short, shard)


def from_partner(shard, axis, apart):
    return lax.ppermute(shard, axis, [(i, i ^ 1 << apart) for i in range(lax.axis_size(axis))])


def ring_gather(piece, axis, during):
    n = lax.axis_size(axis)
    assert n == 4
    cw = [(i, (i + 1) % n) for i in range(n)]
    ccw = [(i, (i - 1) % n) for i in range(n)]
    half = piece.shape[0] // 2
    left = lax.ppermute(piece, axis, cw)
    right = lax.ppermute(piece, axis, ccw)
    left, held = lax.optimization_barrier((left, during()))
    opposite = jnp.concatenate(
        [lax.ppermute(left[:half], axis, cw), lax.ppermute(right[half:], axis, ccw)], axis=0
    )
    return jnp.stack([piece, right, opposite, left]), held


def ring_reduce(parts, axis):
    n = lax.axis_size(axis)
    assert n == 4
    cw = [(i, (i + 1) % n) for i in range(n)]
    ccw = [(i, (i - 1) % n) for i in range(n)]
    half = parts.shape[1] // 2
    f32 = parts.astype(jnp.float32)
    got_a = lax.ppermute(parts[2, :half], axis, cw).astype(jnp.float32)
    got_b = lax.ppermute(parts[2, half:], axis, ccw).astype(jnp.float32)
    to_next = jnp.concatenate([f32[1, :half] + got_a, f32[1, half:]], axis=0)
    to_prev = jnp.concatenate([f32[3, :half], f32[3, half:] + got_b], axis=0)
    from_prev = lax.ppermute(to_next.astype(jnp.bfloat16), axis, cw).astype(jnp.float32)
    from_next = lax.ppermute(to_prev.astype(jnp.bfloat16), axis, ccw).astype(jnp.float32)
    return f32[0] + from_prev + from_next


def on_device(attn, resid, cotangent, gain, numer, pweight, round_bit):
    n_zh = lax.axis_size("zh")
    n_y = lax.axis_size("y")
    n_core = lax.axis_size("core")
    acts = attn[0]
    tok, din = acts.shape
    rows = din // (n_zh * n_y * n_core)
    weight_rows = (numer[0] / pweight[0]).astype(jnp.bfloat16)
    me_c = lax.axis_index("core")
    me_z = lax.axis_index("zh")
    swap_core = [(i, i ^ 1) for i in range(n_core)]
    swap_z = [(i, i ^ 1) for i in range(n_zh)]
    acts5 = acts.reshape(tok, n_zh, n_y, n_core, rows)

    def cols(z, c):
        near = lax.dynamic_index_in_dim(acts5, z, axis=1, keepdims=False)
        return lax.dynamic_index_in_dim(near, c, axis=2, keepdims=False)

    w_near = lax.all_gather(weight_rows, "y", axis=0, tiled=False)
    a_nn, a_no = cols(me_z, me_c), cols(me_z, 1 - me_c)
    me_y = lax.axis_index("y")
    a_fn = jnp.roll(cols(1 - me_z, me_c), -me_y, axis=1)
    a_fo = jnp.roll(cols(1 - me_z, 1 - me_c), -me_y, axis=1)
    w_near, w_cross, a_nn, a_no, a_fn, a_fo = lax.optimization_barrier(
        (w_near, lax.ppermute(weight_rows, "zh", swap_z), a_nn, a_no, a_fn, a_fo)
    )
    w_near_o = lax.ppermute(w_near, "core", swap_core)

    def mm(a, w):
        return jnp.einsum("tyi,yio->to", a, w, preferred_element_type=jnp.float32)

    def near_products():
        pre_near = resid[0].astype(jnp.float32) + mm(a_nn, w_near)
        return pre_near + mm(a_no, w_near_o)

    w_far, pre_near = ring_gather(w_cross, "y", near_products)
    w_far_o = lax.ppermute(w_far, "core", swap_core)
    pre = pre_near + mm(a_fn, w_far) + mm(a_fo, w_far_o)
    inv = lax.rsqrt(jnp.mean(pre * pre, axis=1, keepdims=True) + EPS)
    normed = pre * inv
    dnorm = cotangent[0].astype(jnp.float32) * gain
    dpre = (inv * (dnorm - normed * jnp.mean(dnorm * normed, axis=1, keepdims=True))).astype(
        jnp.bfloat16
    )

    def tm(a):
        return jnp.einsum("tyi,to->yio", a, dpre, preferred_element_type=jnp.float32).astype(
            jnp.bfloat16
        )

    def own_plus_other(a_own, a_other):
        sent = lax.ppermute(tm(a_other), "core", swap_core)
        (own,) = lax.optimization_barrier((tm(a_own),))
        return own + sent

    far = own_plus_other(a_fn, a_fo)
    far = ring_reduce(far, "y").astype(jnp.bfloat16)
    near = own_plus_other(a_nn, a_no)
    near, far = lax.optimization_barrier((near, far))
    far = lax.ppermute(far, "zh", swap_z)
    near = lax.psum_scatter(near, "y", scatter_dimension=0, tiled=False)
    grad = near.astype(jnp.float32) + far.astype(jnp.float32)
    stepped = numer[0] - learning_rate * grad
    levels = lax.axis_size("rep").bit_length() - 1

    def pushed(bit):

        def send(part):
            return from_partner(shortened(part), "rep", bit).astype(part.dtype)

        return send

    def gossip(part):
        return lax.switch(round_bit[0], [pushed(level) for level in range(levels)], part)

    new_pweight = 0.5 * (pweight + gossip(pweight))
    new_numer = (0.5 * (stepped + gossip(stepped)))[None]
    return (new_numer, new_pweight)


def solution(mesh):
    n_rep, n_shard = mesh.devices.shape
    devices = np.asarray(mesh.devices).reshape(n_rep, 2, n_shard // 4, 2)
    split = Mesh(devices, ("rep", "zh", "y", "core"))
    rows = P("rep", ("zh", "y", "core"), None)
    in_specs = (rows, rows, rows, P(), rows, P("rep"), P())
    out_specs = (rows, P("rep"))
    return jax.shard_map(
        on_device, mesh=split, in_specs=in_specs, out_specs=out_specs, check_vma=False
    )
```
